256 devices in a mesh: tok: 8 (over z_hi, core), hid: 32 (over y, x, z_lo).
Axes of the slice: x: 4, y: 4, z: 8 (z_hi: 4, z_lo: 2; z = z_hi * 2 + z_lo), core: 2. Of those that a mesh axis runs over, the one named last changes fastest.
Arguments:
- gate_pre: bfloat16 [1024, 24576], P('tok', 'hid'), may hold values from -6 to 6
- up_pre: bfloat16 [1024, 24576], P('tok', 'hid'), may hold values from -6 to 6
- down_weight: bfloat16 [24576, 6144], P('hid', 'tok'), may hold values from -0.078125 to 0.078125
- residual: bfloat16 [1024, 6144], P('tok', 'hid'), may hold values from -3 to 3
Outputs:
- mixed: bfloat16 [1024, 6144], P('tok', 'hid')
The draws below stay inside these ranges and needn't reach their ends.
All inputs are finite; a program needn't handle non-finite values.
Results may differ from the reference program's by a relative error of at most 0.0043.
Values may be sent and summed in bfloat16 or wider, within the bound.
No kernel may reach another device: no remote copies, remote signals or barrier semaphores. Data moves between devices by JAX's collectives and lax.ppermute only.
A program may use at most 64 MiB of HBM per device.

```python
import jax
import jax.numpy as jnp

D = 6144
FF = 24576
TOKENS = 1024


def strengthened(array, rng, source, target, parts, factor):
    owner, partner = [(jnp.arange(array.shape[dim]) // (array.shape[dim] // parts)).reshape([-1 if axis == dim else 1 for axis in range(array.ndim)]) for dim in (source, target)]
    chosen = jax.random.permutation(rng, parts)[partner]
    strong = (owner == chosen) | (owner == (partner + parts // 2) % parts)
    return jnp.where(strong, factor * array, array)


def level_of(rng, shape, shards, low, top_value):
    loudness = 1.0
    for dim, parts in shards:
        heights = jax.random.uniform(jax.random.fold_in(jax.random.fold_in(rng, 6), dim), (parts,), jnp.float32, low / len(shards), top_value / len(shards))
        loudness = loudness * jnp.repeat(jnp.exp(heights), shape[dim] // parts).reshape((-1,) + (1,) * (len(shape) - 1 - dim))
    return loudness


def bell_draw(key, extent, deviation, most, shards=(), held_as=jnp.bfloat16):
    array = jax.random.normal(key, extent, jnp.float32) * deviation
    if len(shards) > 0:
        array = level_of(key, extent, shards, -0.22, 0.18) * array
    return jnp.clip(array, min=-most, max=most).astype(held_as)


def bell_draw_with(rng, shape, spread, most, cuts, heavy, held_as=jnp.bfloat16):
    values = spread * jax.random.normal(rng, shape, jnp.float32)
    if cuts:
        values = values * level_of(rng, shape, cuts, -0.22, 0.18)
    return jnp.clip(strengthened(values, jax.random.fold_in(rng, 3), *heavy), -most, most).astype(held_as)


def setup_inputs(seed: int = 0) -> dict:
    keys = jax.random.split(jax.random.key(seed), 5)
    return {
        "gate_pre": bell_draw(keys[0], (TOKENS, FF), 1.0, 6.0, ((0, 8), (1, 32))),
        "up_pre": bell_draw(keys[1], (TOKENS, FF), 1.0, 6.0, ((0, 8), (1, 32))),
        "down_weight": bell_draw_with(keys[2], (FF, D), FF ** -0.5, 0.078125, ((0, 32), (1, 8)), (0, 1, 32, 2.75)),
        "residual": bell_draw(keys[3], (TOKENS, D), 0.5, 3.0, ((0, 8), (1, 32))),
    }


def reference(gate_pre, up_pre, down_weight, residual):
    hidden = (jax.nn.silu(gate_pre.astype(jnp.float32)) * up_pre.astype(jnp.float32)).astype(jnp.bfloat16)
    summed = jnp.dot(hidden, down_weight, preferred_element_type=jnp.float32)
    return (summed + residual.astype(jnp.float32)).astype(jnp.bfloat16)
```

```python
import jax
import jax.numpy as jnp
from jax import lax
from jax.sharding import PartitionSpec as P


def swap_pairs(n_tok, n_hid):
    g = n_hid // n_tok
    pairs = []
    for i in range(n_tok):
        for j in range(n_hid):
            pairs.append((i * n_hid + j, (j // g) * n_hid + g * i + j % g))
    return pairs


def per_device(gate_pre, up_pre, down_weight, residual):
    n_tok = lax.axis_size("tok")
    n_hid = lax.axis_size("hid")
    pairs = swap_pairs(n_tok, n_hid)
    res_here = lax.ppermute(residual, ("tok", "hid"), pairs)
    hidden = (jax.nn.silu(gate_pre.astype(jnp.float32)) * up_pre.astype(jnp.float32)).astype(
        jnp.bfloat16
    )
    every_token = jnp.dot(
        lax.all_gather(hidden, "tok", axis=0, tiled=True),
        down_weight,
        preferred_element_type=jnp.float32,
    )
    rows, cols = residual.shape
    g = n_hid // n_tok
    blocks = every_token.reshape(n_tok, rows, g, cols).transpose(0, 2, 1, 3).reshape(n_hid, rows, cols)
    gathered = lax.all_to_all(blocks, "hid", split_axis=0, concat_axis=0, tiled=True)
    summed = gathered.sum(axis=0)
    mixed = (summed + res_here.astype(jnp.float32)).astype(jnp.bfloat16)
    return lax.ppermute(mixed, ("tok", "hid"), pairs)


def solution(mesh):
    in_specs = (P("tok", "hid"), P("tok", "hid"), P("hid", "tok"), P("tok", "hid"))
    out_specs = P("tok", "hid")
    return jax.shard_map(
        per_device, mesh=mesh, in_specs=in_specs, out_specs=out_specs, check_vma=False
    )
```

```python
import jax
import jax.numpy as jnp
from jax import lax
from jax.sharding import Mesh
from jax.sharding import PartitionSpec as P


def arrival_order(t, n_far):
    z, c = divmod(t, 2)
    return [((z - s) % n_far) * 2 + (c if q == 0 else 1 - c) for s in range(n_far) for q in range(2)]


def owner_pairs(n_tok, n_hid):
    g = n_hid // n_tok
    n_far = n_tok // 2
    pairs = []
    for i in range(n_tok):
        order = arrival_order(i, n_far)
        for j in range(n_hid):
            pairs.append((i * n_hid + j, order[j // g] * n_hid + g * i + j % g))
    return pairs


def gather_tokens(hidden, n_far):
    parts = [hidden] + [
        lax.ppermute(hidden, "far", [(a, (a + s) % n_far) for a in range(n_far)])
        for s in range(1, n_far)
    ]
    mine = jnp.stack(parts)
    other = lax.ppermute(mine, "core", [(0, 1), (1, 0)])
    return jnp.stack([mine, other], axis=1).reshape(-1, hidden.shape[1])


def per_device(gate_pre, up_pre, down_weight, residual):
    n_far = lax.axis_size("far")
    n_tok = 2 * n_far
    n_hid = lax.axis_size("hid")
    pairs = owner_pairs(n_tok, n_hid)
    axes = ("far", "core", "hid")
    res_here = lax.ppermute(residual, axes, [(b, a) for a, b in pairs])
    hidden = (jax.nn.silu(gate_pre.astype(jnp.float32)) * up_pre.astype(jnp.float32)).astype(
        jnp.bfloat16
    )
    every_token = jnp.dot(
        gather_tokens(hidden, n_far), down_weight, preferred_element_type=jnp.float32
    )
    rows, cols = residual.shape
    g = n_hid // n_tok
    blocks = every_token.reshape(n_tok, rows, g, cols).transpose(0, 2, 1, 3).reshape(n_hid, rows, cols)
    gathered = lax.all_to_all(blocks, "hid", split_axis=0, concat_axis=0, tiled=True)
    summed = gathered.sum(axis=0)
    mixed = (summed + res_here.astype(jnp.float32)).astype(jnp.bfloat16)
    return lax.ppermute(mixed, axes, pairs)


def solution(mesh):
    n_tok, n_hid = mesh.devices.shape
    split = Mesh(mesh.devices.reshape(n_tok // 2, 2, n_hid), ("far", "core", "hid"))
    tok = ("far", "core")
    in_specs = (P(tok, "hid"), P(tok, "hid"), P("hid", tok), P(tok, "hid"))
    out_specs = P(tok, "hid")
    return jax.shard_map(
        per_device, mesh=split, in_specs=in_specs, out_specs=out_specs, check_vma=False
    )
```

```python
import jax
import jax.numpy as jnp
from jax import lax
from jax.sharding import Mesh
from jax.sharding import PartitionSpec as P

N_CHUNKS = 2


def arrival_order(t, n_far):
    z, c = divmod(t, 2)
    return [((z - s) % n_far) * 2 + (c if q == 0 else 1 - c) for s in range(n_far) for q in range(2)]


def owner_pairs(n_tok, n_hid):
    g = n_hid // n_tok
    n_far = n_tok // 2
    pairs = []
    for i in range(n_tok):
        order = arrival_order(i, n_far)
        for j in range(n_hid):
            pairs.append((i * n_hid + j, order[j // g] * n_hid + g * i + j % g))
    return pairs


def gather_tokens(hidden, n_far):
    parts = [hidden] + [
        lax.ppermute(hidden, "far", [(a, (a + s) % n_far) for a in range(n_far)])
        for s in range(1, n_far)
    ]
    mine = jnp.stack(parts)
    other = lax.ppermute(mine, "core", [(0, 1), (1, 0)])
    return jnp.stack([mine, other], axis=1).reshape(-1, hidden.shape[1])


def per_device(gate_pre, up_pre, down_weight, residual):
    n_far = lax.axis_size("far")
    n_tok = 2 * n_far
    n_hid = lax.axis_size("hid")
    pairs = owner_pairs(n_tok, n_hid)
    axes = ("far", "core", "hid")
    res_here = lax.ppermute(residual, axes, [(b, a) for a, b in pairs])
    hidden = (jax.nn.silu(gate_pre.astype(jnp.float32)) * up_pre.astype(jnp.float32)).astype(
        jnp.bfloat16
    )
    rows, cols = residual.shape
    g = n_hid // n_tok
    step = rows // N_CHUNKS
    sums = []
    for c in range(N_CHUNKS):
        every_token = jnp.dot(
            gather_tokens(hidden[c * step:(c + 1) * step], n_far),
            down_weight,
            preferred_element_type=jnp.float32,
        )
        blocks = every_token.reshape(n_tok, step, g, cols).transpose(0, 2, 1, 3).reshape(n_hid, step, cols)
        gathered = lax.all_to_all(blocks, "hid", split_axis=0, concat_axis=0, tiled=True)
        sums.append(gathered.sum(axis=0))
    summed = jnp.concatenate(sums, axis=0)
    mixed = (summed + res_here.astype(jnp.float32)).astype(jnp.bfloat16)
    return lax.ppermute(mixed, axes, pairs)


def solution(mesh):
    n_tok, n_hid = mesh.devices.shape
    split = Mesh(mesh.devices.reshape(n_tok // 2, 2, n_hid), ("far", "core", "hid"))
    tok = ("far", "core")
    in_specs = (P(tok, "hid"), P(tok, "hid"), P("hid", tok), P(tok, "hid"))
    out_specs = P(tok, "hid")
    return jax.shard_map(
        per_device, mesh=split, in_specs=in_specs, out_specs=out_specs, check_vma=False
    )
```

```python
import jax
import jax.numpy as jnp
from jax import lax
from jax.sharding import Mesh
from jax.sharding import PartitionSpec as P

N_CHUNKS = 1


def arrival_order(t, n_far):
    z, c = divmod(t, 2)
    return [((z - s) % n_far) * 2 + (c if q == 0 else 1 - c) for s in range(n_far) for q in range(2)]


def owner_pairs(n_tok, n_hid):
    g = n_hid // n_tok
    n_far = n_tok // 2
    pairs = []
    for i in range(n_tok):
        order = arrival_order(i, n_far)
        for j in range(n_hid):
            pairs.append((i * n_hid + j, order[j // g] * n_hid + g * i + j % g))
    return pairs


def gather_tokens(hidden, n_far):
    parts = [hidden] + [
        lax.ppermute(hidden, "far", [(a, (a + s) % n_far) for a in range(n_far)])
        for s in range(1, n_far)
    ]
    mine = jnp.stack(parts)
    other = lax.ppermute(mine, "core", [(0, 1), (1, 0)])
    return jnp.stack([mine, other], axis=1).reshape(-1, hidden.shape[1])


def per_device(gate_pre, up_pre, down_weight, residual):
    n_far = lax.axis_size("far")
    n_tok = 2 * n_far
    n_hid = lax.axis_size("hid")
    pairs = owner_pairs(n_tok, n_hid)
    axes = ("far", "core", "hid")
    hidden = (jax.nn.silu(gate_pre.astype(jnp.float32)) * up_pre.astype(jnp.float32)).astype(
        jnp.bfloat16
    )
    rows, cols = residual.shape
    g = n_hid // n_tok
    step = rows // N_CHUNKS
    sums = []
    for c in range(N_CHUNKS):
        every_token = jnp.dot(
            gather_tokens(hidden[c * step:(c + 1) * step], n_far),
            down_weight,
            preferred_element_type=jnp.float32,
        )
        blocks = every_token.reshape(n_tok, step, g, cols).transpose(0, 2, 1, 3).reshape(n_hid, step, cols)
        gathered = lax.all_to_all(blocks, "hid", split_axis=0, concat_axis=0, tiled=True)
        sums.append(gathered.sum(axis=0))
    summed = jnp.concatenate(sums, axis=0)
    owned = lax.ppermute(summed, axes, pairs)
    return (owned + residual.astype(jnp.float32)).astype(jnp.bfloat16)


def solution(mesh):
    n_tok, n_hid = mesh.devices.shape
    split = Mesh(mesh.devices.reshape(n_tok // 2, 2, n_hid), ("far", "core", "hid"))
    tok = ("far", "core")
    in_specs = (P(tok, "hid"), P(tok, "hid"), P("hid", tok), P(tok, "hid"))
    out_specs = P(tok, "hid")
    return jax.shard_map(
        per_device, mesh=split, in_specs=in_specs, out_specs=out_specs, check_vma=False
    )
```

```python
import jax
import jax.numpy as jnp
import numpy as np
from jax import lax
from jax.sharding import Mesh
from jax.sharding import PartitionSpec as P


def ring(d, n):
    d %= n
    return min(d, n - d)


def placement(n_far, n_y):
    piece, token = [], []
    for i in range(2 * n_far):
        z, c = divmod(i, 2)
        pieces = sorted(
            range(2 * n_far), key=lambda m: -2 * ring(m // 2, n_far)
        )
        slots = sorted(
            range(2 * n_far), key=lambda p: ring(p // 2 - z, n_y) + 2 * (p % 2 != c)
        )
        row = [0] * (2 * n_far)
        for p, m in zip(slots, pieces):
            row[p] = m
        piece.append(row)
        token.append([((z - m // 2) % n_far) * 2 + (c if m % 2 == 0 else 1 - c) for m in row])
    return piece, token


def owner_pairs(token, n_tok, n_hid):
    g = n_hid // n_tok
    pairs = []
    for i in range(n_tok):
        for j in range(n_hid):
            pairs.append((i * n_hid + j, token[i][j // g] * n_hid + g * i + j % g))
    return pairs


def gather_tokens(hidden, n_far):
    parts = [hidden] + [
        lax.ppermute(hidden, "far", [(a, (a + s) % n_far) for a in range(n_far)])
        for s in range(1, n_far)
    ]
    mine = jnp.stack(parts)
    other = lax.ppermute(mine, "core", [(0, 1), (1, 0)])
    return jnp.stack([mine, other], axis=1).reshape(2 * n_far, *hidden.shape)


def per_device(gate_pre, up_pre, down_weight, residual):
    n_far = lax.axis_size("far")
    n_tok = 2 * n_far
    n_hid = lax.axis_size("hid")
    g = n_hid // n_tok
    piece, token = placement(n_far, n_hid // (g * 2))
    pairs = owner_pairs(token, n_tok, n_hid)
    axes = ("far", "core", "hid")
    hidden = (jax.nn.silu(gate_pre.astype(jnp.float32)) * up_pre.astype(jnp.float32)).astype(
        jnp.bfloat16
    )
    rows, cols = residual.shape
    pieces = gather_tokens(hidden, n_far)
    here = jnp.asarray(np.array(piece, np.int32))[lax.axis_index(("far", "core"))]
    placed = jnp.take(pieces, here, axis=0).reshape(n_tok * rows, -1)
    every_token = jnp.dot(placed, down_weight, preferred_element_type=jnp.float32)
    blocks = every_token.reshape(n_tok, rows, g, cols).transpose(0, 2, 1, 3).reshape(n_hid, rows, cols)
    gathered = lax.all_to_all(blocks, "hid", split_axis=0, concat_axis=0, tiled=True)
    summed = gathered.sum(axis=0)
    owned = lax.ppermute(summed, axes, pairs)
    return (owned + residual.astype(jnp.float32)).astype(jnp.bfloat16)


def solution(mesh):
    n_tok, n_hid = mesh.devices.shape
    split = Mesh(mesh.devices.reshape(n_tok // 2, 2, n_hid), ("far", "core", "hid"))
    tok = ("far", "core")
    in_specs = (P(tok, "hid"), P(tok, "hid"), P("hid", tok), P(tok, "hid"))
    out_specs = P(tok, "hid")
    return jax.shard_map(
        per_device, mesh=split, in_specs=in_specs, out_specs=out_specs, check_vma=False
    )
```

```python
import jax
import jax.numpy as jnp
import numpy as np
from jax import lax
from jax.sharding import Mesh
from jax.sharding import PartitionSpec as P


def ring(d, n):
    d %= n
    return min(d, n - d)


def placement(n_far, n_y):
    piece, token = [], []
    for i in range(2 * n_far):
        z, c = divmod(i, 2)
        pieces = sorted(
            range(2 * n_far), key=lambda m: -2 * ring(m // 2 - z, n_far)
        )
        slots = sorted(
            range(2 * n_far), key=lambda p: ring(p // 2 - z, n_y) + 2 * (p % 2 != c)
        )
        row = [0] * (2 * n_far)
        for p, m in zip(slots, pieces):
            row[p] = m
        piece.append(row)
        token.append([(m // 2) * 2 + (c if m % 2 == 0 else 1 - c) for m in row])
    return piece, token


def owner_pairs(token, n_tok, n_hid):
    g = n_hid // n_tok
    pairs = []
    for i in range(n_tok):
        for j in range(n_hid):
            pairs.append((i * n_hid + j, token[i][j // g] * n_hid + g * i + j % g))
    return pairs


def gather_tokens(hidden):
    mine = lax.all_gather(hidden, "far", axis=0, tiled=False)
    other = lax.ppermute(mine, "core", [(0, 1), (1, 0)])
    return jnp.stack([mine, other], axis=1).reshape(-1, *hidden.shape)


def per_device(gate_pre, up_pre, down_weight, residual):
    n_far = lax.axis_size("far")
    n_tok = 2 * n_far
    n_hid = lax.axis_size("hid")
    g = n_hid // n_tok
    piece, token = placement(n_far, n_hid // (g * 2))
    pairs = owner_pairs(token, n_tok, n_hid)
    axes = ("far", "core", "hid")
    hidden = (jax.nn.silu(gate_pre.astype(jnp.float32)) * up_pre.astype(jnp.float32)).astype(
        jnp.bfloat16
    )
    rows, cols = residual.shape
    pieces = gather_tokens(hidden)
    here = jnp.asarray(np.array(piece, np.int32))[lax.axis_index(("far", "core"))]
    placed = jnp.take(pieces, here, axis=0).reshape(n_tok * rows, -1)
    every_token = jnp.dot(placed, down_weight, preferred_element_type=jnp.float32)
    blocks = every_token.reshape(n_tok, rows, g, cols).transpose(0, 2, 1, 3).reshape(n_hid, rows, cols)
    gathered = lax.all_to_all(blocks, "hid", split_axis=0, concat_axis=0, tiled=True)
    summed = gathered.sum(axis=0)
    owned = lax.ppermute(summed, axes, pairs)
    return (owned + residual.astype(jnp.float32)).astype(jnp.bfloat16)


def solution(mesh):
    n_tok, n_hid = mesh.devices.shape
    split = Mesh(mesh.devices.reshape(n_tok // 2, 2, n_hid), ("far", "core", "hid"))
    tok = ("far", "core")
    in_specs = (P(tok, "hid"), P(tok, "hid"), P("hid", tok), P(tok, "hid"))
    out_specs = P(tok, "hid")
    return jax.shard_map(
        per_device, mesh=split, in_specs=in_specs, out_specs=out_specs, check_vma=False
    )
```

```python
import jax
import jax.numpy as jnp
import numpy as np
from jax import lax
from jax.sharding import Mesh
from jax.sharding import PartitionSpec as P


def ring(d, n):
    d %= n
    return min(d, n - d)


def placement(n_far, n_y):
    piece, token = [], []
    for i in range(2 * n_far):
        z, c = divmod(i, 2)
        pieces = sorted(
            range(2 * n_far), key=lambda m: -2 * ring(m // 2 - z, n_far)
        )
        slots = sorted(
            range(2 * n_far), key=lambda p: ring(p // 2 - z, n_y) + 2 * (p % 2 != c)
        )
        row = [0] * (2 * n_far)
        for p, m in zip(slots, pieces):
            row[p] = m
        piece.append(row)
        token.append([(m // 2) * 2 + (c if m % 2 == 0 else 1 - c) for m in row])
    return piece, token


def owner_pairs(token, n_tok, n_hid):
    g = n_hid // n_tok
    pairs = []
    for i in range(n_tok):
        for j in range(n_hid):
            pairs.append((i * n_hid + j, token[i][j // g] * n_hid + g * i + j % g))
    return pairs


def gather_tokens(hidden):
    mine = lax.all_gather(hidden, "far", axis=0, tiled=False)
    other = lax.ppermute(mine, "core", [(0, 1), (1, 0)])
    return jnp.stack([mine, other], axis=1).reshape(-1, *hidden.shape)


def per_device(gate_pre, up_pre, down_weight, residual):
    n_far = lax.axis_size("far")
    n_tok = 2 * n_far
    n_zl = lax.axis_size("zl")
    n_hid = lax.axis_size("yx") * n_zl
    g = n_hid // n_tok
    piece, token = placement(n_far, n_hid // (g * 2))
    pairs = owner_pairs(token, n_tok, n_hid)
    owner = dict(pairs)
    axes = ("far", "core", "yx", "zl")
    hidden = (jax.nn.silu(gate_pre.astype(jnp.float32)) * up_pre.astype(jnp.float32)).astype(
        jnp.bfloat16
    )
    rows, cols = residual.shape
    pieces = gather_tokens(hidden)
    here = jnp.asarray(np.array(piece, np.int32))[lax.axis_index(("far", "core"))]
    placed = jnp.take(pieces, here, axis=0).reshape(n_tok * rows, -1)
    every_token = jnp.dot(placed, down_weight, preferred_element_type=jnp.float32)
    blocks = every_token.reshape(n_tok, rows, g, cols).transpose(0, 2, 1, 3)
    blocks = blocks.reshape(n_hid // n_zl, n_zl, rows, cols)
    half = lax.all_to_all(blocks, "yx", split_axis=0, concat_axis=0, tiled=True).sum(axis=0)
    zl = lax.axis_index("zl")
    total = None
    for d in range(n_zl):
        part = lax.dynamic_index_in_dim(half, (zl + d) % n_zl, axis=0, keepdims=False)
        moved = lax.ppermute(
            part, axes, [(a, owner[a - a % n_zl + (a % n_zl + d) % n_zl]) for a in range(len(pairs))]
        )
        total = moved if total is None else total + moved
    return (total + residual.astype(jnp.float32)).astype(jnp.bfloat16)


def solution(mesh):
    n_tok, n_hid = mesh.devices.shape
    split = Mesh(mesh.devices.reshape(n_tok // 2, 2, n_hid // 2, 2), ("far", "core", "yx", "zl"))
    tok = ("far", "core")
    hid = ("yx", "zl")
    in_specs = (P(tok, hid), P(tok, hid), P(hid, tok), P(tok, hid))
    out_specs = P(tok, hid)
    return jax.shard_map(
        per_device, mesh=split, in_specs=in_specs, out_specs=out_specs, check_vma=False
    )
```

```python
import jax
import jax.numpy as jnp
import numpy as np
from jax import lax
from jax.sharding import Mesh
from jax.sharding import PartitionSpec as P


def ring(d, n):
    d %= n
    return min(d, n - d)


def placement(n_far, n_y):
    piece, token = [], []
    for i in range(2 * n_far):
        z, c = divmod(i, 2)
        pieces = sorted(
            range(2 * n_far), key=lambda m: -2 * ring(m // 2 - z, n_far)
        )
        slots = sorted(
            range(2 * n_far), key=lambda p: ring(p // 2 - z, n_y) + 2 * (p % 2 != c)
        )
        row = [0] * (2 * n_far)
        for p, m in zip(slots, pieces):
            row[p] = m
        piece.append(row)
        token.append([(m // 2) * 2 + (c if m % 2 == 0 else 1 - c) for m in row])
    return piece, token


def owner_pairs(token, n_tok, n_hid):
    g = n_hid // n_tok
    pairs = []
    for i in range(n_tok):
        for j in range(n_hid):
            pairs.append((i * n_hid + j, token[i][j // g] * n_hid + g * i + j % g))
    return pairs


def gather_tokens(hidden):
    mine = lax.all_gather(hidden, "far", axis=0, tiled=False)
    other = lax.ppermute(mine, "core", [(0, 1), (1, 0)])
    return jnp.stack([mine, other], axis=1).reshape(-1, *hidden.shape)


def per_device(gate_pre, up_pre, down_weight, residual):
    n_far = lax.axis_size("far")
    n_tok = 2 * n_far
    n_hid = lax.axis_size("hid")
    g = n_hid // n_tok
    piece, token = placement(n_far, n_hid // (g * 2))
    pairs = owner_pairs(token, n_tok, n_hid)
    axes = ("far", "core", "hid")
    hidden = (jax.nn.silu(gate_pre.astype(jnp.float32)) * up_pre.astype(jnp.float32)).astype(
        jnp.bfloat16
    )
    rows, cols = residual.shape
    here = jnp.asarray(np.array(piece, np.int32))[lax.axis_index(("far", "core"))]
    hidden, weight_t, here = lax.optimization_barrier((hidden, down_weight.T, here))
    pieces = gather_tokens(hidden)
    placed = pieces.at[here].get(mode="promise_in_bounds").reshape(n_tok * rows, -1)
    every_token = jnp.dot(placed, weight_t.T, preferred_element_type=jnp.float32)
    blocks = every_token.reshape(n_tok, rows, g, cols).transpose(0, 2, 1, 3).reshape(n_hid, rows, cols)
    gathered = lax.all_to_all(blocks, "hid", split_axis=0, concat_axis=0, tiled=True)
    summed = gathered.sum(axis=0)
    owned = lax.ppermute(summed, axes, pairs)
    return (owned + residual.astype(jnp.float32)).astype(jnp.bfloat16)


def solution(mesh):
    n_tok, n_hid = mesh.devices.shape
    split = Mesh(mesh.devices.reshape(n_tok // 2, 2, n_hid), ("far", "core", "hid"))
    tok = ("far", "core")
    in_specs = (P(tok, "hid"), P(tok, "hid"), P("hid", tok), P(tok, "hid"))
    out_specs = P(tok, "hid")
    return jax.shard_map(
        per_device, mesh=split, in_specs=in_specs, out_specs=out_specs, check_vma=False
    )
```

```python
import jax
import jax.numpy as jnp
import numpy as np
from jax import lax
from jax.sharding import Mesh
from jax.sharding import PartitionSpec as P


def ring(d, n):
    d %= n
    return min(d, n - d)


def placement(n_far, n_y):
    piece, token = [], []
    for i in range(2 * n_far):
        z, c = divmod(i, 2)
        pieces = sorted(
            range(2 * n_far), key=lambda m: -2 * ring(m // 2 - z, n_far)
        )
        slots = sorted(
            range(2 * n_far), key=lambda p: ring(p // 2 - z, n_y) + 2 * (p % 2 != c)
        )
        row = [0] * (2 * n_far)
        for p, m in zip(slots, pieces):
            row[p] = m
        piece.append(row)
        token.append([(m // 2) * 2 + (c if m % 2 == 0 else 1 - c) for m in row])
    return piece, token


def owner_pairs(token, n_tok, n_hid):
    g = n_hid // n_tok
    pairs = []
    for i in range(n_tok):
        for j in range(n_hid):
            pairs.append((i * n_hid + j, token[i][j // g] * n_hid + g * i + j % g))
    return pairs


def gather_tokens(hidden):
    mine = lax.all_gather(hidden, "far", axis=0, tiled=False)
    other = lax.ppermute(mine, "core", [(0, 1), (1, 0)])
    return jnp.stack([mine, other], axis=1).reshape(-1, *hidden.shape)


def per_device(gate_pre, up_pre, down_weight, residual):
    n_far = lax.axis_size("far")
    n_tok = 2 * n_far
    n_hid = lax.axis_size("hid")
    g = n_hid // n_tok
    piece, token = placement(n_far, n_hid // (g * 2))
    pairs = owner_pairs(token, n_tok, n_hid)
    axes = ("far", "core", "hid")
    hidden = (jax.nn.silu(gate_pre.astype(jnp.float32)) * up_pre.astype(jnp.float32)).astype(
        jnp.bfloat16
    )
    rows, cols = residual.shape
    here = jnp.asarray(np.array(piece, np.int32))[lax.axis_index(("far", "core"))]
    step = rows // 2
    sums = []
    for c in range(2):
        pieces = gather_tokens(hidden[c * step:(c + 1) * step])
        placed = jnp.take(pieces, here, axis=0).reshape(n_tok * step, -1)
        every_token = jnp.dot(placed, down_weight, preferred_element_type=jnp.float32)
        blocks = every_token.reshape(n_tok, step, g, cols).transpose(0, 2, 1, 3).reshape(n_hid, step, cols)
        gathered = lax.all_to_all(blocks, "hid", split_axis=0, concat_axis=0, tiled=True)
        sums.append(gathered.sum(axis=0))
    summed = jnp.concatenate(sums, axis=0)
    owned = lax.ppermute(summed, axes, pairs)
    return (owned + residual.astype(jnp.float32)).astype(jnp.bfloat16)


def solution(mesh):
    n_tok, n_hid = mesh.devices.shape
    split = Mesh(mesh.devices.reshape(n_tok // 2, 2, n_hid), ("far", "core", "hid"))
    tok = ("far", "core")
    in_specs = (P(tok, "hid"), P(tok, "hid"), P("hid", tok), P(tok, "hid"))
    out_specs = P(tok, "hid")
    return jax.shard_map(
        per_device, mesh=split, in_specs=in_specs, out_specs=out_specs, check_vma=False
    )
```

```python
import jax
import jax.numpy as jnp
import numpy as np
from jax import lax
from jax.sharding import Mesh
from jax.sharding import PartitionSpec as P


def ring(d, n):
    d %= n
    return min(d, n - d)


def placement(n_far, n_y):
    piece, token = [], []
    for i in range(2 * n_far):
        z, c = divmod(i, 2)
        pieces = sorted(
            range(2 * n_far), key=lambda m: -2 * ring(m // 2 - z, n_far)
        )
        slots = sorted(
            range(2 * n_far), key=lambda p: ring(p // 2 - z, n_y) + 2 * (p % 2 != c)
        )
        row = [0] * (2 * n_far)
        for p, m in zip(slots, pieces):
            row[p] = m
        piece.append(row)
        token.append([(m // 2) * 2 + (c if m % 2 == 0 else 1 - c) for m in row])
    return piece, token


def owner_pairs(token, n_tok, n_hid):
    g = n_hid // n_tok
    pairs = []
    for i in range(n_tok):
        for j in range(n_hid):
            pairs.append((i * n_hid + j, token[i][j // g] * n_hid + g * i + j % g))
    return pairs


def gather_tokens(hidden):
    mine = lax.all_gather(hidden, "far", axis=0, tiled=False)
    other = lax.ppermute(mine, "core", [(0, 1), (1, 0)])
    return jnp.stack([mine, other], axis=1).reshape(-1, *hidden.shape)


def per_device(gate_pre, up_pre, down_weight, residual):
    n_far = lax.axis_size("far")
    n_tok = 2 * n_far
    n_hid = lax.axis_size("hid")
    g = n_hid // n_tok
    piece, token = placement(n_far, n_hid // (g * 2))
    pairs = owner_pairs(token, n_tok, n_hid)
    axes = ("far", "core", "hid")
    hidden = (jax.nn.silu(gate_pre.astype(jnp.float32)) * up_pre.astype(jnp.float32)).astype(
        jnp.bfloat16
    )
    rows, cols = residual.shape
    res_here = lax.ppermute(residual, axes, [(b, a) for a, b in pairs])
    hidden, res_here = lax.optimization_barrier((hidden, res_here))
    pieces = gather_tokens(hidden)
    here = jnp.asarray(np.array(piece, np.int32))[lax.axis_index(("far", "core"))]
    placed = jnp.take(pieces, here, axis=0).reshape(n_tok * rows, -1)
    every_token = jnp.dot(placed, down_weight, preferred_element_type=jnp.float32)
    blocks = every_token.reshape(n_tok, rows, g, cols).transpose(0, 2, 1, 3).reshape(n_hid, rows, cols)
    gathered = lax.all_to_all(blocks, "hid", split_axis=0, concat_axis=0, tiled=True)
    summed = gathered.sum(axis=0)
    mixed = (summed + res_here.astype(jnp.float32)).astype(jnp.bfloat16)
    return lax.ppermute(mixed, axes, pairs)


def solution(mesh):
    n_tok, n_hid = mesh.devices.shape
    split = Mesh(mesh.devices.reshape(n_tok // 2, 2, n_hid), ("far", "core", "hid"))
    tok = ("far", "core")
    in_specs = (P(tok, "hid"), P(tok, "hid"), P("hid", tok), P(tok, "hid"))
    out_specs = P(tok, "hid")
    return jax.shard_map(
        per_device, mesh=split, in_specs=in_specs, out_specs=out_specs, check_vma=False
    )
```

```python
import jax
import jax.numpy as jnp
import numpy as np
from jax import lax
from jax.sharding import Mesh
from jax.sharding import PartitionSpec as P


def ring(d, n):
    d %= n
    return min(d, n - d)


def placement(n_far, n_y):
    piece, token = [], []
    for i in range(2 * n_far):
        z, c = divmod(i, 2)
        pieces = sorted(
            range(2 * n_far), key=lambda m: -2 * ring(m // 2 - z, n_far)
        )
        slots = sorted(
            range(2 * n_far), key=lambda p: ring(p // 2 - z, n_y) + 2 * (p % 2 != c)
        )
        row = [0] * (2 * n_far)
        for p, m in zip(slots, pieces):
            row[p] = m
        piece.append(row)
        token.append([(m // 2) * 2 + (c if m % 2 == 0 else 1 - c) for m in row])
    return piece, token


def owner_pairs(token, n_tok, n_hid):
    g = n_hid // n_tok
    pairs = []
    for i in range(n_tok):
        for j in range(n_hid):
            pairs.append((i * n_hid + j, token[i][j // g] * n_hid + g * i + j % g))
    return pairs


def gather_tokens(hidden):
    mine = lax.all_gather(hidden, "far", axis=0, tiled=False)
    other = lax.ppermute(mine, "core", [(0, 1), (1, 0)])
    return jnp.stack([mine, other], axis=1).reshape(-1, *hidden.shape)


def per_device(gate_pre, up_pre, down_weight, residual):
    n_far = lax.axis_size("far")
    n_tok = 2 * n_far
    n_hid = lax.axis_size("hid")
    g = n_hid // n_tok
    piece, token = placement(n_far, n_hid // (g * 2))
    pairs = owner_pairs(token, n_tok, n_hid)
    axes = ("far", "core", "hid")
    hidden = (jax.nn.silu(gate_pre.astype(jnp.float32)) * up_pre.astype(jnp.float32)).astype(
        jnp.bfloat16
    )
    rows, cols = residual.shape
    pieces = gather_tokens(hidden)
    here = jnp.asarray(np.array(piece, np.int32))[lax.axis_index(("far", "core"))]
    placed = pieces.at[here].get(mode="promise_in_bounds").reshape(n_tok * rows, -1)
    every_token = jnp.dot(placed, down_weight, preferred_element_type=jnp.float32)
    blocks = every_token.reshape(n_tok, rows, g, cols).transpose(0, 2, 1, 3).reshape(n_hid, rows, cols)
    gathered = lax.all_to_all(blocks, "hid", split_axis=0, concat_axis=0, tiled=True)
    summed = gathered.sum(axis=0)
    owned = lax.ppermute(summed, axes, pairs)
    return (owned + residual.astype(jnp.float32)).astype(jnp.bfloat16)


def solution(mesh):
    n_tok, n_hid = mesh.devices.shape
    split = Mesh(mesh.devices.reshape(n_tok // 2, 2, n_hid), ("far", "core", "hid"))
    tok = ("far", "core")
    in_specs = (P(tok, "hid"), P(tok, "hid"), P("hid", tok), P(tok, "hid"))
    out_specs = P(tok, "hid")
    return jax.shard_map(
        per_device, mesh=split, in_specs=in_specs, out_specs=out_specs, check_vma=False
    )
```

```python
import jax
import jax.numpy as jnp
from jax import lax
from jax.sharding import Mesh
from jax.sharding import PartitionSpec as P


def arrival_order(n_far):
    return [
        [f * 2 + (c if q == 0 else 1 - c) for f in range(n_far) for q in range(2)]
        for z in range(n_far)
        for c in range(2)
    ]


def owner_pairs(token, n_tok, n_hid):
    g = n_hid // n_tok
    pairs = []
    for i in range(n_tok):
        for j in range(n_hid):
            pairs.append((i * n_hid + j, token[i][j // g] * n_hid + g * i + j % g))
    return pairs


def gather_tokens(hidden):
    mine = lax.all_gather(hidden, "far", axis=0, tiled=False)
    other = lax.ppermute(mine, "core", [(0, 1), (1, 0)])
    return jnp.stack([mine, other], axis=1).reshape(-1, *hidden.shape)


def per_device(gate_pre, up_pre, down_weight, residual):
    n_far = lax.axis_size("far")
    n_tok = 2 * n_far
    n_hid = lax.axis_size("hid")
    g = n_hid // n_tok
    token = arrival_order(n_far)
    pairs = owner_pairs(token, n_tok, n_hid)
    axes = ("far", "core", "hid")
    hidden = (jax.nn.silu(gate_pre.astype(jnp.float32)) * up_pre.astype(jnp.float32)).astype(
        jnp.bfloat16
    )
    rows, cols = residual.shape
    pieces = gather_tokens(hidden)
    placed = pieces.reshape(n_tok * rows, -1)
    every_token = jnp.dot(placed, down_weight, preferred_element_type=jnp.float32)
    blocks = every_token.reshape(n_tok, rows, g, cols).transpose(0, 2, 1, 3).reshape(n_hid, rows, cols)
    gathered = lax.all_to_all(blocks, "hid", split_axis=0, concat_axis=0, tiled=True)
    summed = gathered.sum(axis=0)
    owned = lax.ppermute(summed, axes, pairs)
    return (owned + residual.astype(jnp.float32)).astype(jnp.bfloat16)


def solution(mesh):
    n_tok, n_hid = mesh.devices.shape
    split = Mesh(mesh.devices.reshape(n_tok // 2, 2, n_hid), ("far", "core", "hid"))
    tok = ("far", "core")
    in_specs = (P(tok, "hid"), P(tok, "hid"), P("hid", tok), P(tok, "hid"))
    out_specs = P(tok, "hid")
    return jax.shard_map(
        per_device, mesh=split, in_specs=in_specs, out_specs=out_specs, check_vma=False
    )
```

```python
import jax
import jax.numpy as jnp
import numpy as np
from jax import lax
from jax.sharding import Mesh
from jax.sharding import PartitionSpec as P


def ring(d, n):
    d %= n
    return min(d, n - d)


def placement(n_far, n_y):
    piece, token = [], []
    for i in range(2 * n_far):
        z, c = divmod(i, 2)
        pieces = sorted(
            range(2 * n_far), key=lambda m: -2 * ring(m // 2 - z, n_far)
        )
        slots = sorted(
            range(2 * n_far), key=lambda p: ring(p // 2 - z, n_y) + 2 * (p % 2 != c)
        )
        row = [0] * (2 * n_far)
        for p, m in zip(slots, pieces):
            row[p] = m
        piece.append(row)
        token.append([(m // 2) * 2 + (c if m % 2 == 0 else 1 - c) for m in row])
    return piece, token


def owner_pairs(token, n_tok, n_hid):
    g = n_hid // n_tok
    pairs = []
    for i in range(n_tok):
        for j in range(n_hid):
            pairs.append((i * n_hid + j, token[i][j // g] * n_hid + g * i + j % g))
    return pairs


def gather_tokens(hidden):
    mine = lax.all_gather(hidden, "far", axis=0, tiled=False)
    other = lax.ppermute(mine, "core", [(0, 1), (1, 0)])
    return jnp.stack([mine, other], axis=1).reshape(-1, *hidden.shape)


def per_device(gate_pre, up_pre, down_weight, residual):
    n_far = lax.axis_size("far")
    n_tok = 2 * n_far
    n_y, n_x, n_zl = (lax.axis_size(a) for a in ("y", "x", "zl"))
    n_hid = n_y * n_x * n_zl
    g = n_hid // n_tok
    piece, token = placement(n_far, n_hid // (g * 2))
    pairs = owner_pairs(token, n_tok, n_hid)
    axes = ("far", "core", "y", "x", "zl")
    hidden = (jax.nn.silu(gate_pre.astype(jnp.float32)) * up_pre.astype(jnp.float32)).astype(
        jnp.bfloat16
    )
    rows, cols = residual.shape
    pieces = gather_tokens(hidden)
    here = jnp.asarray(np.array(piece, np.int32))[lax.axis_index(("far", "core"))]
    placed = pieces.at[here].get(mode="promise_in_bounds").reshape(n_tok * rows, -1)
    every_token = jnp.dot(placed, down_weight, preferred_element_type=jnp.float32)
    blocks = every_token.reshape(n_tok, rows, g, cols).transpose(0, 2, 1, 3)
    blocks = blocks.reshape(n_y, n_x, n_zl, rows, cols).transpose(2, 0, 1, 3, 4).reshape(n_hid, rows, cols)
    gathered = lax.all_to_all(blocks, ("zl", "y", "x"), split_axis=0, concat_axis=0, tiled=True)
    summed = gathered.sum(axis=0)
    owned = lax.ppermute(summed, axes, pairs)
    return (owned + residual.astype(jnp.float32)).astype(jnp.bfloat16)


def solution(mesh):
    n_tok, n_hid = mesh.devices.shape
    split = Mesh(
        mesh.devices.reshape(n_tok // 2, 2, 4, 4, n_hid // 16), ("far", "core", "y", "x", "zl")
    )
    tok = ("far", "core")
    hid = ("y", "x", "zl")
    in_specs = (P(tok, hid), P(tok, hid), P(hid, tok), P(tok, hid))
    out_specs = P(tok, hid)
    return jax.shard_map(
        per_device, mesh=split, in_specs=in_specs, out_specs=out_specs, check_vma=False
    )
```
